1024 devices in a mesh: gx: 32 (over x, z_hi, core), gy: 32 (over y, z_lo).
Axes of the slice: x: 8, y: 8, z: 8 (z_hi: 2, z_lo: 4; z = z_hi * 4 + z_lo), core: 2. Of those that a mesh axis runs over, the one named last changes fastest.
Arguments:
- flow_state: float32 [20, 128, 192, 128], P(None, 'gx', 'gy'), may hold values from -6 to 6
- reacting: int32 [128, 192], P('gx', 'gy'), may hold values from 0 to 1, as said below
- w_in: bfloat16 [20, 1600], replicated, may hold values from -1.25 to 1.25
- w_mid: bfloat16 [1600, 800], replicated, may hold values from -0.15625 to 0.15625
- w_low: bfloat16 [800, 400], replicated, may hold values from -0.21875 to 0.21875
- w_out: bfloat16 [20, 400], replicated, may hold values from -0.3125 to 0.3125
- diffusivity: float32 [20], replicated, may hold values from 0.1 to 1
Outputs:
- new_state: float32 [20, 128, 192, 128], P(None, 'gx', 'gy')
The draws below stay inside these ranges and needn't reach their ends.
Inputs may be any that keep to these rules, and one draw needn't show every extreme that they name: Tiles are the 4 x 6 blocks of columns whose first indices start at multiples of 4 and 6. In every band of 6 columns along the second dimension that starts at a multiple of 6, exactly 288 columns react; every tile holds between 0 and 18 reacting columns, its count differing from 9 by at least 5, and in every band some tile holds 18 and some tile 0. In the first band, the first 16 tiles along the first dimension hold 18 each and the others 0 each.
All inputs are finite; a program needn't handle non-finite values.
Results may differ from the reference program's by a relative error of at most 0.00055.
Values may be sent and summed in bfloat16 or wider, within the bound.
No kernel may reach another device: no remote copies, remote signals or barrier semaphores. Data moves between devices by JAX's collectives and lax.ppermute only.
A program may use at most 32 MiB of HBM per device.

```python
import math
import jax
import jax.numpy as jnp
from jax import lax

NF = 20
H1 = 1600
H2 = 800
H3 = 400
CX = 4
CY = 6
CZ = 128
NX = 128
NY = 192
SHARE = 9
N_GX = 32
N_GY = 32


def draw_reacting(key, part):
    tiles_x = NX // CX
    tiles_y = NY // CY
    tile_blocks = CX * CY
    share_count = 3 * tile_blocks // 8
    spread = min(share_count, tile_blocks - share_count)
    half_tiles = tiles_x // 2
    key_order, key_excess, key_cells = jax.random.split(key, 3)
    order_score = jax.random.randint(key_order, (tiles_y, tiles_x), 0, 4 * tiles_x).astype(jnp.int32) * tiles_x + jnp.arange(tiles_x, dtype=jnp.int32)[None, :]
    permuted = jnp.argsort(order_score, axis=1, stable=True).astype(jnp.int32)
    inverse = jnp.argsort(permuted, axis=1, stable=True).astype(jnp.int32)
    first_band = (jnp.arange(tiles_y, dtype=jnp.int32) == 0)[:, None]
    inverse = jnp.where(first_band, jnp.arange(tiles_x, dtype=jnp.int32)[None, :], inverse).astype(jnp.int32)
    excess = jax.random.randint(key_excess, (tiles_y, half_tiles), (spread + 1) // 2, spread + 1).astype(jnp.int32)
    excess = excess.at[:, 0].set(spread)
    excess = jnp.where(first_band, jnp.int32(spread), excess).astype(jnp.int32)
    by_place = jnp.concatenate([share_count + excess, share_count - excess], axis=1)
    tile_counts = jnp.take_along_axis(by_place, inverse, axis=1)
    cell_score = jax.random.randint(key_cells, (tiles_y, tiles_x, tile_blocks), 0, 64).astype(jnp.int32) * tile_blocks + jnp.arange(tile_blocks, dtype=jnp.int32)[None, None, :]
    cell_order = jnp.argsort(cell_score, axis=2, stable=True).astype(jnp.int32)
    cell_rank = jnp.argsort(cell_order, axis=2, stable=True).astype(jnp.int32)
    marked = (cell_rank < tile_counts[:, :, None]).astype(jnp.int32)
    react_grid = marked.reshape(tiles_y, tiles_x, CX, CY).transpose(1, 2, 0, 3).reshape(NX, NY)
    return react_grid.astype(jnp.int32)


def level_of(own_key, dims, shards, least, largest):
    gain, own = 1.0, jax.random.fold_in(own_key, 6)
    for axis_at, shards_of in shards:
        heights = jnp.exp(jax.random.uniform(jax.random.fold_in(own, axis_at), (shards_of,), jnp.float32, least / len(shards), largest / len(shards)))
        gain = gain * jnp.repeat(heights, dims[axis_at] // shards_of).reshape([-1 if axis == axis_at else 1 for axis in range(len(dims))])
    return gain


def gaussian(key, shape, deviation, most, pieces=(), kind=jnp.bfloat16):
    loudness = level_of(key, shape, pieces, -0.22, 0.18) if pieces else 1.0
    drawn = jax.random.normal(key, shape, jnp.float32) * deviation * loudness
    return jnp.minimum(jnp.maximum(drawn, -most), most).astype(kind)


def setup_inputs(seed: int = 0) -> dict:
    seeds = jax.random.split(jax.random.key(seed), 8)
    return {
        "flow_state": gaussian(seeds[0], (NF, NX, NY, CZ), 1.0, 6.0, ((1, 32), (2, 32)), jnp.float32),
        "reacting": draw_reacting(jax.random.fold_in(seeds[7], 71), 0),
        "w_in": gaussian(seeds[2], (NF, H1), NF ** -0.5, 1.25),
        "w_mid": gaussian(seeds[3], (H1, H2), H1 ** -0.5, 0.15625),
        "w_low": gaussian(seeds[4], (H2, H3), H2 ** -0.5, 0.21875),
        "w_out": gaussian(seeds[5], (NF, H3), H3 ** -0.5, 0.3125),
        "diffusivity": jnp.clip(jnp.exp(jax.random.uniform(seeds[6], (NF,), jnp.float32, math.log(0.1), math.log(1.0))), 0.1, 1.0),
    }


step_size = 0.05
reaction_gain = 8.0
velocity_x = 1.0
velocity_y = -0.6
velocity_z = 0.35


def stencil(shifted):
    plus_one = shifted(1)
    plus_two = shifted(2)
    minus_one = shifted(-1)
    minus_two = shifted(-2)
    slope = (8.0 * (plus_one - minus_one) - (plus_two - minus_two)) / 12.0
    curve = (16.0 * (plus_one + minus_one) - (plus_two + minus_two) - 30.0 * shifted(0)) / 12.0
    return slope, curve


def transport(field_set, diffusivity):
    slope_x, curve_x = stencil(lambda step_k: jnp.roll(field_set, -step_k, axis=1))
    slope_y, curve_y = stencil(lambda step_k: jnp.roll(field_set, -step_k, axis=2))
    slope_z, curve_z = stencil(lambda step_k: jnp.roll(field_set, -step_k, axis=3))
    return -(velocity_x * slope_x + velocity_y * slope_y + velocity_z * slope_z) + diffusivity[:, None, None, None] * (curve_x + curve_y + curve_z)


def network_rows(cell_rows, w_in, w_mid, w_low, w_out):
    hidden = jax.nn.silu(jnp.dot(cell_rows, w_in, preferred_element_type=jnp.float32)).astype(jnp.bfloat16)
    hidden = jax.nn.silu(jnp.dot(hidden, w_mid, preferred_element_type=jnp.float32)).astype(jnp.bfloat16)
    hidden = jax.nn.silu(jnp.dot(hidden, w_low, preferred_element_type=jnp.float32)).astype(jnp.bfloat16)
    return jnp.dot(hidden, w_out.T, preferred_element_type=jnp.float32).astype(jnp.bfloat16)


def chemistry(field_set, columns, w_in, w_mid, w_low, w_out):
    fields = field_set.shape[0]
    reacting_total = columns.shape[0]
    flattened = field_set.reshape(fields, NX * NY, CZ)
    picked = jnp.take(flattened, columns, axis=1)
    picked = jnp.transpose(picked, (1, 2, 0)).astype(jnp.bfloat16)
    picked = picked.reshape(N_GX, reacting_total // N_GX, CZ, fields)

    def per_group(group_rows):
        return network_rows(group_rows.reshape(-1, fields), w_in, w_mid, w_low, w_out).reshape(group_rows.shape)

    results = lax.map(per_group, picked).reshape(reacting_total, CZ, fields).astype(jnp.float32)
    scattered = jnp.zeros((NX * NY, CZ, fields), jnp.float32).at[columns].set(results)
    return jnp.transpose(scattered, (2, 0, 1)).reshape(fields, NX, NY, CZ)


def reference(flow_state, reacting, w_in, w_mid, w_low, w_out, diffusivity):
    columns = jnp.nonzero(reacting.reshape(-1) == 1, size=SHARE * N_GX * N_GY)[0].astype(jnp.int32)
    reaction = chemistry(flow_state, columns, w_in, w_mid, w_low, w_out)

    def tendency(field_set):
        return transport(field_set, diffusivity) + reaction_gain * reaction

    first_section = flow_state + step_size * tendency(flow_state)
    return 0.5 * flow_state + 0.5 * (first_section + step_size * tendency(first_section))
```

```python
import jax
import jax.numpy as jnp
from jax import lax
from jax.sharding import PartitionSpec as P

step_size = 0.05
reaction_gain = 8.0
velocity_x = 1.0
velocity_y = -0.6
velocity_z = 0.35


def padded_2(x, sides, width):
    for axis, dim in sides:
        peers, length = (lax.axis_size(axis), x.shape[dim])
        up = [(i, (i + 1) % peers) for i in range(peers)]
        down = [(j, i) for i, j in up]
        last = lax.slice_in_dim(x, length - width, length, axis=dim)
        leading = lax.slice_in_dim(x, 0, width, axis=dim)
        before = lax.ppermute(last, axis, up)
        after = lax.ppermute(leading, axis, down)
        x = jnp.concatenate([before, x, after], axis=dim)
    return x


def stencil(shifted):
    plus_one = shifted(1)
    plus_two = shifted(2)
    minus_one = shifted(-1)
    minus_two = shifted(-2)
    slope = (8.0 * (plus_one - minus_one) - (plus_two - minus_two)) / 12.0
    curve = (16.0 * (plus_one + minus_one) - (plus_two + minus_two) - 30.0 * shifted(0)) / 12.0
    return (slope, curve)


def transport(field_set, diffusivity):
    wide_x = field_set.shape[1]
    wide_y = field_set.shape[2]
    padded = padded_2(field_set.astype(jnp.bfloat16), (("gx", 1), ("gy", 2)), 2).astype(
        field_set.dtype
    )
    slope_x, curve_x = stencil(
        lambda step_k: padded[:, 2 + step_k : 2 + step_k + wide_x, 2 : 2 + wide_y, :]
    )
    slope_y, curve_y = stencil(
        lambda step_k: padded[:, 2 : 2 + wide_x, 2 + step_k : 2 + step_k + wide_y, :]
    )
    slope_z, curve_z = stencil(lambda step_k: jnp.roll(field_set, -step_k, axis=3))
    return -(velocity_x * slope_x + velocity_y * slope_y + velocity_z * slope_z) + diffusivity[
        :, None, None, None
    ] * (curve_x + curve_y + curve_z)


def network(cell_rows, w_in, w_mid, w_low, w_out):
    hidden = jax.nn.silu(
        jnp.einsum("bfz,fh->bzh", cell_rows, w_in, preferred_element_type=jnp.float32)
    ).astype(jnp.bfloat16)
    hidden = jax.nn.silu(
        jnp.einsum("bzh,hk->bzk", hidden, w_mid, preferred_element_type=jnp.float32)
    ).astype(jnp.bfloat16)
    hidden = jax.nn.silu(
        jnp.einsum("bzk,kj->bzj", hidden, w_low, preferred_element_type=jnp.float32)
    ).astype(jnp.bfloat16)
    return jnp.einsum("bzj,fj->bfz", hidden, w_out, preferred_element_type=jnp.float32).astype(
        jnp.bfloat16
    )


def body(flow_state, reacting, w_in, w_mid, w_low, w_out, diffusivity):
    fields, wide_x, wide_y, depth_z = flow_state.shape
    blocks = wide_x * wide_y
    share = 3 * blocks // 8
    spread = min(share, blocks - share)
    cap = min(blocks, share + spread)
    live_mask = reacting.reshape(blocks)
    local_rank = jnp.cumsum(live_mask) - live_mask
    keep_pick = (
        (local_rank[None, :] == jnp.arange(cap)[:, None]) & (live_mask[None, :] == 1)
    ).astype(jnp.bfloat16)
    rows = jnp.moveaxis(flow_state.reshape(fields, blocks, depth_z), 1, 0).astype(jnp.bfloat16)
    batch = jnp.einsum("qb,bfz->qfz", keep_pick, rows, preferred_element_type=jnp.float32).astype(
        jnp.bfloat16
    )
    results = network(batch, w_in, w_mid, w_low, w_out)
    source = jnp.einsum("qb,qfz->bfz", keep_pick, results, preferred_element_type=jnp.float32)
    reaction = jnp.moveaxis(source, 0, 1).reshape(fields, wide_x, wide_y, depth_z)

    def tendency(field_set):
        return transport(field_set, diffusivity) + reaction_gain * reaction

    first_section = flow_state + step_size * tendency(flow_state)
    return 0.5 * flow_state + 0.5 * (first_section + step_size * tendency(first_section))


def solution(mesh):
    in_specs = (P(None, "gx", "gy", None), P("gx", "gy"), P(), P(), P(), P(), P())
    out_specs = P(None, "gx", "gy", None)
    return jax.shard_map(body, mesh=mesh, in_specs=in_specs, out_specs=out_specs, check_vma=False)
```

```python
import jax
import jax.numpy as jnp
import numpy as np
from jax import lax
from jax.sharding import PartitionSpec as P

step_size = 0.05
reaction_gain = 8.0
velocity_x = 1.0
velocity_y = -0.6
velocity_z = 0.35


def ring(axis, step):
    peers = lax.axis_size(axis)
    return [(i, (i + step) % peers) for i in range(peers)]


def halos(x):
    wide_x, wide_y = x.shape[1], x.shape[2]
    low = x.astype(jnp.bfloat16)
    x_before = lax.ppermute(low[:, wide_x - 2 :], "gx", ring("gx", 1))
    x_after = lax.ppermute(low[:, :2], "gx", ring("gx", -1))
    y_before = lax.ppermute(low[:, :, wide_y - 2 :], "gy", ring("gy", 1))
    y_after = lax.ppermute(low[:, :, :2], "gy", ring("gy", -1))
    return x_before, x_after, y_before, y_after


def circulant(depth, taps):
    m = np.zeros((depth, depth), np.float32)
    for k, c in taps.items():
        for z in range(depth):
            m[(z + k) % depth, z] += c
    return jnp.asarray(m)


def stencil(shifted):
    plus_one = shifted(1)
    plus_two = shifted(2)
    minus_one = shifted(-1)
    minus_two = shifted(-2)
    slope = (8.0 * (plus_one - minus_one) - (plus_two - minus_two)) / 12.0
    curve = (16.0 * (plus_one + minus_one) - (plus_two + minus_two) - 30.0 * shifted(0)) / 12.0
    return (slope, curve)


def transport(field_set, diffusivity):
    wide_x = field_set.shape[1]
    wide_y = field_set.shape[2]
    depth = field_set.shape[3]
    x_before, x_after, y_before, y_after = halos(field_set)
    dtype = field_set.dtype
    pad_x = jnp.concatenate([x_before.astype(dtype), field_set, x_after.astype(dtype)], axis=1)
    pad_y = jnp.concatenate([y_before.astype(dtype), field_set, y_after.astype(dtype)], axis=2)
    slope_x, curve_x = stencil(lambda k: pad_x[:, 2 + k : 2 + k + wide_x])
    slope_y, curve_y = stencil(lambda k: pad_y[:, :, 2 + k : 2 + k + wide_y])
    slope_m = circulant(depth, {1: 8.0, -1: -8.0, 2: -1.0, -2: 1.0})
    curve_m = circulant(depth, {1: 16.0, -1: 16.0, 2: -1.0, -2: -1.0, 0: -30.0})
    slope_z = jnp.einsum("fxyz,zw->fxyw", field_set, slope_m, precision=lax.Precision.HIGHEST) / 12.0
    curve_z = jnp.einsum("fxyz,zw->fxyw", field_set, curve_m, precision=lax.Precision.HIGHEST) / 12.0
    return -(velocity_x * slope_x + velocity_y * slope_y + velocity_z * slope_z) + diffusivity[
        :, None, None, None
    ] * (curve_x + curve_y + curve_z)


def network(cell_rows, w_in, w_mid, w_low, w_out):
    hidden = jax.nn.silu(
        jnp.einsum("bfz,fh->bzh", cell_rows, w_in, preferred_element_type=jnp.float32)
    ).astype(jnp.bfloat16)
    hidden = jax.nn.silu(
        jnp.einsum("bzh,hk->bzk", hidden, w_mid, preferred_element_type=jnp.float32)
    ).astype(jnp.bfloat16)
    hidden = jax.nn.silu(
        jnp.einsum("bzk,kj->bzj", hidden, w_low, preferred_element_type=jnp.float32)
    ).astype(jnp.bfloat16)
    return jnp.einsum("bzj,fj->bfz", hidden, w_out, preferred_element_type=jnp.float32).astype(
        jnp.bfloat16
    )


def body(flow_state, reacting, w_in, w_mid, w_low, w_out, diffusivity):
    fields, wide_x, wide_y, depth_z = flow_state.shape
    blocks = wide_x * wide_y
    share = 3 * blocks // 8
    spread = min(share, blocks - share)
    cap = min(blocks, share + spread)
    live_mask = reacting.reshape(blocks)
    order = jnp.arange(blocks)
    local_rank = jnp.sum(jnp.where(order[None, :] < order[:, None], live_mask[None, :], 0), axis=1)
    keep_pick = (
        (local_rank[None, :] == jnp.arange(cap)[:, None]) & (live_mask[None, :] == 1)
    ).astype(jnp.bfloat16)
    rows = jnp.moveaxis(flow_state.reshape(fields, blocks, depth_z), 1, 0).astype(jnp.bfloat16)
    batch = jnp.einsum("qb,bfz->qfz", keep_pick, rows, preferred_element_type=jnp.float32).astype(
        jnp.bfloat16
    )
    results = network(batch, w_in, w_mid, w_low, w_out)
    source = jnp.einsum("qb,qfz->bfz", keep_pick, results, preferred_element_type=jnp.float32)
    reaction = jnp.moveaxis(source, 0, 1).reshape(fields, wide_x, wide_y, depth_z)

    def tendency(field_set):
        return transport(field_set, diffusivity) + reaction_gain * reaction

    first_section = flow_state + step_size * tendency(flow_state)
    return 0.5 * flow_state + 0.5 * (first_section + step_size * tendency(first_section))


def solution(mesh):
    in_specs = (P(None, "gx", "gy", None), P("gx", "gy"), P(), P(), P(), P(), P())
    out_specs = P(None, "gx", "gy", None)
    return jax.shard_map(body, mesh=mesh, in_specs=in_specs, out_specs=out_specs, check_vma=False)
```

```python
import jax
import jax.numpy as jnp
import numpy as np
from jax import lax
from jax.sharding import PartitionSpec as P

step_size = 0.05
reaction_gain = 8.0
velocity_x = 1.0
velocity_y = -0.6
velocity_z = 0.35


def ring(axis, step):
    peers = lax.axis_size(axis)
    return [(i, (i + step) % peers) for i in range(peers)]


def halos(x):
    wide_x, wide_y = x.shape[1], x.shape[2]
    low = jnp.bfloat16
    x_before = lax.ppermute(x[:, wide_x - 2 :].astype(low), "gx", ring("gx", 1))
    x_after = lax.ppermute(x[:, :2].astype(low), "gx", ring("gx", -1))
    y_before = lax.ppermute(x[:, :, wide_y - 2 :].astype(low), "gy", ring("gy", 1))
    y_after = lax.ppermute(x[:, :, :2].astype(low), "gy", ring("gy", -1))
    return x_before, x_after, y_before, y_after


def circulant(depth, taps):
    m = np.zeros((depth, depth), np.float32)
    for k, c in taps.items():
        for z in range(depth):
            m[(z + k) % depth, z] += c
    return jnp.asarray(m)


def stencil(shifted):
    plus_one = shifted(1)
    plus_two = shifted(2)
    minus_one = shifted(-1)
    minus_two = shifted(-2)
    slope = (8.0 * (plus_one - minus_one) - (plus_two - minus_two)) / 12.0
    curve = (16.0 * (plus_one + minus_one) - (plus_two + minus_two) - 30.0 * shifted(0)) / 12.0
    return (slope, curve)


def transport(field_set, diffusivity):
    wide_x = field_set.shape[1]
    wide_y = field_set.shape[2]
    depth = field_set.shape[3]
    x_before, x_after, y_before, y_after = halos(field_set)
    dtype = field_set.dtype
    pad_x = jnp.concatenate([x_before.astype(dtype), field_set, x_after.astype(dtype)], axis=1)
    pad_y = jnp.concatenate([y_before.astype(dtype), field_set, y_after.astype(dtype)], axis=2)
    slope_x, curve_x = stencil(lambda k: pad_x[:, 2 + k : 2 + k + wide_x])
    slope_y, curve_y = stencil(lambda k: pad_y[:, :, 2 + k : 2 + k + wide_y])
    slope_m = circulant(depth, {1: 8.0, -1: -8.0, 2: -1.0, -2: 1.0})
    curve_m = circulant(depth, {1: 16.0, -1: 16.0, 2: -1.0, -2: -1.0, 0: -30.0})
    slope_z = jnp.einsum("fxyz,zw->fxyw", field_set, slope_m, precision=lax.Precision.HIGH) / 12.0
    curve_z = jnp.einsum("fxyz,zw->fxyw", field_set, curve_m, precision=lax.Precision.HIGH) / 12.0
    return -(velocity_x * slope_x + velocity_y * slope_y + velocity_z * slope_z) + diffusivity[
        :, None, None, None
    ] * (curve_x + curve_y + curve_z)


def network(cell_rows, w_in, w_mid, w_low, w_out):
    hidden = jax.nn.silu(
        jnp.einsum("bfz,fh->bzh", cell_rows, w_in, preferred_element_type=jnp.float32)
    ).astype(jnp.bfloat16)
    hidden = jax.nn.silu(
        jnp.einsum("bzh,hk->bzk", hidden, w_mid, preferred_element_type=jnp.float32)
    ).astype(jnp.bfloat16)
    hidden = jax.nn.silu(
        jnp.einsum("bzk,kj->bzj", hidden, w_low, preferred_element_type=jnp.float32)
    ).astype(jnp.bfloat16)
    return jnp.einsum("bzj,fj->bfz", hidden, w_out, preferred_element_type=jnp.float32).astype(
        jnp.bfloat16
    )


def body(flow_state, reacting, w_in, w_mid, w_low, w_out, diffusivity):
    fields, wide_x, wide_y, depth_z = flow_state.shape
    blocks = wide_x * wide_y
    share = 3 * blocks // 8
    spread = min(share, blocks - share)
    cap = min(blocks, share + spread)
    live_mask = reacting.reshape(blocks)
    order = jnp.arange(blocks)
    local_rank = jnp.sum(jnp.where(order[None, :] < order[:, None], live_mask[None, :], 0), axis=1)
    keep_pick = (
        (local_rank[None, :] == jnp.arange(cap)[:, None]) & (live_mask[None, :] == 1)
    ).astype(jnp.bfloat16)
    rows = jnp.moveaxis(flow_state.reshape(fields, blocks, depth_z), 1, 0).astype(jnp.bfloat16)
    batch = jnp.einsum("qb,bfz->qfz", keep_pick, rows, preferred_element_type=jnp.float32).astype(
        jnp.bfloat16
    )
    results = network(batch, w_in, w_mid, w_low, w_out)
    source = jnp.einsum("qb,qfz->bfz", keep_pick, results, preferred_element_type=jnp.float32)
    reaction = jnp.moveaxis(source, 0, 1).reshape(fields, wide_x, wide_y, depth_z)

    def tendency(field_set):
        return transport(field_set, diffusivity) + reaction_gain * reaction

    first_section = flow_state + step_size * tendency(flow_state)
    return 0.5 * flow_state + 0.5 * (first_section + step_size * tendency(first_section))


def solution(mesh):
    in_specs = (P(None, "gx", "gy", None), P("gx", "gy"), P(), P(), P(), P(), P())
    out_specs = P(None, "gx", "gy", None)
    return jax.shard_map(body, mesh=mesh, in_specs=in_specs, out_specs=out_specs, check_vma=False)
```

```python
import jax
import jax.numpy as jnp
import numpy as np
from jax import lax
from jax.sharding import PartitionSpec as P

step_size = 0.05
reaction_gain = 8.0
velocity_x = 1.0
velocity_y = -0.6
velocity_z = 0.35


def ring(axis, step):
    peers = lax.axis_size(axis)
    return [(i, (i + step) % peers) for i in range(peers)]


def swap_faces(first, last, axis):
    peers = lax.axis_size(axis)
    if peers % 2:
        before = lax.ppermute(last, axis, ring(axis, 1))
        after = lax.ppermute(first, axis, ring(axis, -1))
        return before, after
    even = lax.axis_index(axis) % 2 == 0
    outer = [(i, (i + 1) % peers) for i in range(1, peers, 2)]
    outer = outer + [(j, i) for i, j in outer]
    inner = [(i, i + 1) for i in range(0, peers, 2)]
    inner = inner + [(j, i) for i, j in inner]
    got_outer = lax.ppermute(jnp.where(even, first, last), axis, outer)
    got_inner = lax.ppermute(jnp.where(even, last, first), axis, inner)
    before = jnp.where(even, got_outer, got_inner)
    after = jnp.where(even, got_inner, got_outer)
    return before, after


def halos(x):
    wide_x, wide_y = x.shape[1], x.shape[2]
    low = jnp.bfloat16
    x_before, x_after = swap_faces(x[:, :2].astype(low), x[:, wide_x - 2 :].astype(low), "gx")
    y_before, y_after = swap_faces(x[:, :, :2].astype(low), x[:, :, wide_y - 2 :].astype(low), "gy")
    return x_before, x_after, y_before, y_after


def circulant(depth, taps):
    m = np.zeros((depth, depth), np.float32)
    for k, c in taps.items():
        for z in range(depth):
            m[(z + k) % depth, z] += c
    return jnp.asarray(m)


def stencil(shifted):
    plus_one = shifted(1)
    plus_two = shifted(2)
    minus_one = shifted(-1)
    minus_two = shifted(-2)
    slope = (8.0 * (plus_one - minus_one) - (plus_two - minus_two)) / 12.0
    curve = (16.0 * (plus_one + minus_one) - (plus_two + minus_two) - 30.0 * shifted(0)) / 12.0
    return (slope, curve)


def transport(field_set, diffusivity):
    wide_x = field_set.shape[1]
    wide_y = field_set.shape[2]
    depth = field_set.shape[3]
    x_before, x_after, y_before, y_after = halos(field_set)
    dtype = field_set.dtype
    pad_x = jnp.concatenate([x_before.astype(dtype), field_set, x_after.astype(dtype)], axis=1)
    pad_y = jnp.concatenate([y_before.astype(dtype), field_set, y_after.astype(dtype)], axis=2)
    slope_x, curve_x = stencil(lambda k: pad_x[:, 2 + k : 2 + k + wide_x])
    slope_y, curve_y = stencil(lambda k: pad_y[:, :, 2 + k : 2 + k + wide_y])
    slope_m = circulant(depth, {1: 8.0, -1: -8.0, 2: -1.0, -2: 1.0})
    curve_m = circulant(depth, {1: 16.0, -1: 16.0, 2: -1.0, -2: -1.0, 0: -30.0})
    both = jnp.einsum(
        "fxyz,zw->fxyw",
        field_set,
        jnp.concatenate([slope_m, curve_m], axis=1),
        precision=lax.Precision.HIGH,
    )
    slope_z = both[..., :depth] / 12.0
    curve_z = both[..., depth:] / 12.0
    return -(velocity_x * slope_x + velocity_y * slope_y + velocity_z * slope_z) + diffusivity[
        :, None, None, None
    ] * (curve_x + curve_y + curve_z)


def network(cell_rows, w_in, w_mid, w_low, w_out):
    hidden = jax.nn.silu(
        jnp.einsum("bfz,fh->bzh", cell_rows, w_in, preferred_element_type=jnp.float32)
    ).astype(jnp.bfloat16)
    hidden = jax.nn.silu(
        jnp.einsum("bzh,hk->bzk", hidden, w_mid, preferred_element_type=jnp.float32)
    ).astype(jnp.bfloat16)
    hidden = jax.nn.silu(
        jnp.einsum("bzk,kj->bzj", hidden, w_low, preferred_element_type=jnp.float32)
    ).astype(jnp.bfloat16)
    return jnp.einsum("bzj,fj->bfz", hidden, w_out, preferred_element_type=jnp.float32).astype(
        jnp.bfloat16
    )


def body(flow_state, reacting, w_in, w_mid, w_low, w_out, diffusivity):
    fields, wide_x, wide_y, depth_z = flow_state.shape
    blocks = wide_x * wide_y
    share = 3 * blocks // 8
    spread = min(share, blocks - share)
    cap = min(blocks, share + spread)
    live = reacting == 1
    flat = jnp.arange(blocks).reshape(wide_x, wide_y)
    earlier = flat[None, None, :, :] < flat[:, :, None, None]
    local_rank = jnp.sum(jnp.where(earlier & live[None, None, :, :], 1, 0), axis=(2, 3))
    keep_pick = (
        (local_rank[None, :, :] == jnp.arange(cap)[:, None, None]) & live[None, :, :]
    ).astype(jnp.bfloat16)
    batch = jnp.einsum(
        "qxy,fxyz->qfz", keep_pick, flow_state.astype(jnp.bfloat16), preferred_element_type=jnp.float32
    ).astype(jnp.bfloat16)
    results = network(batch, w_in, w_mid, w_low, w_out)
    reaction = jnp.einsum("qxy,qfz->fxyz", keep_pick, results, preferred_element_type=jnp.float32)

    def tendency(field_set):
        return transport(field_set, diffusivity) + reaction_gain * reaction

    first_section = flow_state + step_size * tendency(flow_state)
    return 0.5 * flow_state + 0.5 * (first_section + step_size * tendency(first_section))


def solution(mesh):
    in_specs = (P(None, "gx", "gy", None), P("gx", "gy"), P(), P(), P(), P(), P())
    out_specs = P(None, "gx", "gy", None)
    return jax.shard_map(body, mesh=mesh, in_specs=in_specs, out_specs=out_specs, check_vma=False)
```
